256 devices in a mesh: embed: 8 (over x, core), hidden: 32 (over y, z).
Axes of the slice: x: 4, y: 4, z: 8, core: 2. Of those that a mesh axis runs over, the one named last changes fastest.
Arguments:
- rows_in: bfloat16 [512, 16384], P('hidden', 'embed'), may hold values from -6 to 6
- gate_weight: bfloat16 [16384, 28672], P('embed', 'hidden'), may hold values from -0.046875 to 0.046875
- up_weight: bfloat16 [16384, 28672], P('embed', 'hidden'), may hold values from -0.046875 to 0.046875
- down_weight: bfloat16 [28672, 16384], P('hidden', 'embed'), may hold values from -0.03125 to 0.03125
Outputs:
- rows_out: bfloat16 [512, 16384], P('hidden', 'embed')
The draws below stay inside these ranges and needn't reach their ends.
All inputs are finite; a program needn't handle non-finite values.
Results may differ from the reference program's by a relative error of at most 0.0049.
Values may be sent and summed in bfloat16 or wider, within the bound.
No kernel may reach another device: no remote copies, remote signals or barrier semaphores. Data moves between devices by JAX's collectives and lax.ppermute only.
A program may use at most 64 MiB of HBM per device.

```python
import jax
import jax.numpy as jnp

D = 16384
FFW = 28672
ROWS = 512


def shard_levels(rng, dims, split, low, largest):
    gain = 1.0
    for position, blocks in split:
        steps = jax.random.uniform(jax.random.fold_in(jax.random.fold_in(rng, 6), position), (blocks,), jnp.float32, low / len(split), largest / len(split))
        gain = gain * jnp.repeat(jnp.exp(steps), dims[position] // blocks).reshape((-1,) + (1,) * (len(dims) - 1 - position))
    return gain


def gaussian(own_key, shape, deviation, most, split=(), held_as=jnp.bfloat16):
    drawn = deviation * jax.random.normal(own_key, shape, jnp.float32)
    if split:
        drawn = drawn * shard_levels(own_key, shape, split, -0.22, 0.18)
    return jnp.clip(drawn, -most, most).astype(held_as)


def setup_inputs(seed: int = 0) -> dict:
    arg_keys = jax.random.split(jax.random.key(seed), 5)
    return {
        "rows_in": gaussian(arg_keys[0], (ROWS, D), 1.0, 6.0, ((0, 32), (1, 8))),
        "gate_weight": gaussian(arg_keys[1], (D, FFW), D ** -0.5, 0.046875, ((0, 8), (1, 32))),
        "up_weight": gaussian(arg_keys[2], (D, FFW), D ** -0.5, 0.046875, ((0, 8), (1, 32))),
        "down_weight": gaussian(arg_keys[3], (FFW, D), FFW ** -0.5, 0.03125, ((0, 32), (1, 8))),
    }


def reference(rows_in, gate_weight, up_weight, down_weight):
    gate = jnp.dot(rows_in, gate_weight, preferred_element_type=jnp.float32)
    up = jnp.dot(rows_in, up_weight, preferred_element_type=jnp.float32)
    act = (jax.nn.silu(gate) * up).astype(jnp.bfloat16)
    return jnp.dot(act, down_weight, preferred_element_type=jnp.float32).astype(jnp.bfloat16)
```

```python
import jax
import jax.numpy as jnp
from jax import lax
from jax.sharding import Mesh, PartitionSpec as P


def on_device(rows_in, gate_weight, up_weight, down_weight):
    width = gate_weight.shape[1]
    piece = lax.all_gather(rows_in, "hz", axis=0, tiled=True)
    piece = lax.all_gather(piece, "hy", axis=0, tiled=True)
    gate_part = jnp.dot(piece, gate_weight, preferred_element_type=jnp.float32)
    up_part = jnp.dot(piece, up_weight, preferred_element_type=jnp.float32)
    partial_value = jnp.concatenate([gate_part, up_part], axis=1)
    summed = lax.psum_scatter(partial_value, "embed", scatter_dimension=0, tiled=True)
    activated = (jax.nn.silu(summed[:, :width]) * summed[:, width:]).astype(jnp.bfloat16)
    activated = lax.all_gather(activated, "embed", axis=0, tiled=True)
    partial_out = jnp.dot(activated, down_weight, preferred_element_type=jnp.float32)
    totals = lax.psum_scatter(partial_out, "hy", scatter_dimension=0, tiled=True)
    totals = lax.psum_scatter(totals, "hz", scatter_dimension=0, tiled=True)
    return totals.astype(jnp.bfloat16)


def solution(mesh):
    embed, hidden = mesh.shape["embed"], mesh.shape["hidden"]
    ny = {d.coords[1] for d in mesh.devices.flat}
    ny = len(ny)
    sub = Mesh(mesh.devices.reshape(embed, ny, hidden // ny), ("embed", "hy", "hz"))
    rows = P(("hy", "hz"), "embed")
    weights = P("embed", ("hy", "hz"))
    placed = (rows, weights, weights, P(("hy", "hz"), "embed"))
    return jax.shard_map(
        on_device, mesh=sub, in_specs=placed, out_specs=rows, check_vma=False
    )
```

```python
import jax
import jax.numpy as jnp
from jax import lax
from jax.sharding import Mesh, PartitionSpec as P


def on_device(rows_in, gate_weight, up_weight, down_weight):
    width = gate_weight.shape[1]
    piece = lax.all_gather(rows_in, "hz", axis=0, tiled=True)
    piece = lax.all_gather(piece, "hy", axis=0, tiled=True)
    gate_part = jnp.dot(piece, gate_weight, preferred_element_type=jnp.float32)
    up_part = jnp.dot(piece, up_weight, preferred_element_type=jnp.float32)
    partial_value = jnp.concatenate([gate_part, up_part], axis=1)
    summed = lax.psum_scatter(partial_value, "embed", scatter_dimension=0, tiled=True)
    activated = (jax.nn.silu(summed[:, :width]) * summed[:, width:]).astype(jnp.bfloat16)
    activated = lax.all_gather(activated, "embed", axis=0, tiled=True)
    partial_out = jnp.dot(activated, down_weight, preferred_element_type=jnp.float32)
    owners = lax.psum(1, ("hy", "hz"))
    pieces = partial_out.astype(jnp.bfloat16).reshape(
        (owners, partial_out.shape[0] // owners) + partial_out.shape[1:]
    )
    pieces = lax.all_to_all(pieces, ("hy", "hz"), 0, 0, tiled=True)
    totals = pieces.astype(jnp.float32).sum(axis=0)
    return totals.astype(jnp.bfloat16)


def solution(mesh):
    embed, hidden = mesh.shape["embed"], mesh.shape["hidden"]
    ny = {d.coords[1] for d in mesh.devices.flat}
    ny = len(ny)
    sub = Mesh(mesh.devices.reshape(embed, ny, hidden // ny), ("embed", "hy", "hz"))
    rows = P(("hy", "hz"), "embed")
    weights = P("embed", ("hy", "hz"))
    placed = (rows, weights, weights, P(("hy", "hz"), "embed"))
    return jax.shard_map(
        on_device, mesh=sub, in_specs=placed, out_specs=rows, check_vma=False
    )
```

```python
import jax
import jax.numpy as jnp
from jax import lax
from jax.sharding import Mesh, PartitionSpec as P


def on_device(rows_in, gate_weight, up_weight, down_weight):
    width = gate_weight.shape[1]
    piece = lax.all_gather(rows_in, "hy", axis=0, tiled=True)
    piece = lax.all_gather(piece, "hz", axis=0, tiled=True)
    piece = piece.reshape((-1, rows_in.shape[0]) + piece.shape[1:])
    piece = piece.reshape((lax.psum(1, "hz"), lax.psum(1, "hy")) + piece.shape[1:])
    piece = jnp.swapaxes(piece, 0, 1).reshape((-1,) + rows_in.shape[1:])
    gate_part = jnp.dot(piece, gate_weight, preferred_element_type=jnp.float32)
    up_part = jnp.dot(piece, up_weight, preferred_element_type=jnp.float32)
    partial_value = jnp.concatenate([gate_part, up_part], axis=1)
    summed = lax.psum_scatter(partial_value, "embed", scatter_dimension=0, tiled=True)
    activated = (jax.nn.silu(summed[:, :width]) * summed[:, width:]).astype(jnp.bfloat16)
    activated = lax.all_gather(activated, "embed", axis=0, tiled=True)
    partial_out = jnp.dot(activated, down_weight, preferred_element_type=jnp.float32)
    owners = lax.psum(1, ("hy", "hz"))
    pieces = partial_out.astype(jnp.bfloat16).reshape(
        (owners, partial_out.shape[0] // owners) + partial_out.shape[1:]
    )
    pieces = lax.all_to_all(pieces, ("hy", "hz"), 0, 0, tiled=True)
    totals = pieces.astype(jnp.float32).sum(axis=0)
    return totals.astype(jnp.bfloat16)


def solution(mesh):
    embed, hidden = mesh.shape["embed"], mesh.shape["hidden"]
    ny = {d.coords[1] for d in mesh.devices.flat}
    ny = len(ny)
    sub = Mesh(mesh.devices.reshape(embed, ny, hidden // ny), ("embed", "hy", "hz"))
    rows = P(("hy", "hz"), "embed")
    weights = P("embed", ("hy", "hz"))
    placed = (rows, weights, weights, P(("hy", "hz"), "embed"))
    return jax.shard_map(
        on_device, mesh=sub, in_specs=placed, out_specs=rows, check_vma=False
    )
```

```python
import jax
import jax.numpy as jnp
from jax import lax
from jax.sharding import Mesh, PartitionSpec as P

EMBED = ("ex", "ec")


def ring_rs(x, axis, n):
    k = lax.axis_index(axis)
    xs = x.reshape((n, x.shape[0] // n) + x.shape[1:])
    half = x.shape[-1] // 2
    a, b = xs[..., :half], xs[..., half:]
    take = lambda arr, i: lax.dynamic_index_in_dim(arr, i % n, 0, keepdims=False)
    fwd = [(i, (i + 1) % n) for i in range(n)]
    bwd = [(i, (i - 1) % n) for i in range(n)]
    acc_a = take(a, k - 1)
    acc_b = take(b, k + 1)
    for s in range(n - 1):
        acc_a = lax.ppermute(acc_a, axis, fwd) + take(a, k - s - 2)
        acc_b = lax.ppermute(acc_b, axis, bwd) + take(b, k + s + 2)
    return jnp.concatenate([acc_a, acc_b], axis=-1)


def ring_ag(x, axis, n):
    k = lax.axis_index(axis)
    fwd = [(i, (i + 1) % n) for i in range(n)]
    bwd = [(i, (i - 1) % n) for i in range(n)]
    nf = n // 2
    out = jnp.zeros((n,) + x.shape, x.dtype)
    put = lambda out, v, i: lax.dynamic_update_index_in_dim(out, v, i % n, 0)
    out = put(out, x, k)
    buf = x
    for s in range(nf):
        buf = lax.ppermute(buf, axis, fwd)
        out = put(out, buf, k - 1 - s)
    buf = x
    for s in range(n - 1 - nf):
        buf = lax.ppermute(buf, axis, bwd)
        out = put(out, buf, k + 1 + s)
    return out.reshape((n * x.shape[0],) + x.shape[1:])


def embed_rs(x):
    ec = lax.axis_index("ec")
    ncore = lax.psum(1, "ec")
    nx = lax.psum(1, "ex")
    xs = x.reshape((nx, ncore, x.shape[0] // (nx * ncore)) + x.shape[1:])
    mine = lax.dynamic_index_in_dim(xs, ec, 1, keepdims=False)
    other = lax.dynamic_index_in_dim(xs, 1 - ec, 1, keepdims=False)
    got = lax.ppermute(other, "ec", [(0, 1), (1, 0)])
    y = (mine + got).reshape((-1,) + x.shape[1:])
    return ring_rs(y, "ex", nx)


def on_device(rows_in, gate_weight, up_weight, down_weight):
    width = gate_weight.shape[1]
    ny = lax.psum(1, "hy")
    nz = lax.psum(1, "hz")
    piece = ring_ag(ring_ag(rows_in, "hy", ny), "hz", nz)
    gate_part = jnp.dot(piece, gate_weight, preferred_element_type=jnp.float32)
    up_part = jnp.dot(piece, up_weight, preferred_element_type=jnp.float32)
    partial_value = jnp.concatenate([gate_part, up_part], axis=1)
    summed = embed_rs(partial_value)
    activated = (jax.nn.silu(summed[:, :width]) * summed[:, width:]).astype(jnp.bfloat16)
    activated = lax.all_gather(activated, EMBED, axis=0, tiled=True)
    partial_out = jnp.dot(activated, down_weight, preferred_element_type=jnp.float32)
    pieces = partial_out.astype(jnp.bfloat16).reshape(
        (ny * nz, partial_out.shape[0] // (ny * nz)) + partial_out.shape[1:]
    )
    pieces = lax.all_to_all(pieces, ("hz", "hy"), 0, 0, tiled=True)
    totals = pieces.astype(jnp.float32).sum(axis=0)
    return totals.astype(jnp.bfloat16)


def solution(mesh):
    embed, hidden = mesh.shape["embed"], mesh.shape["hidden"]
    nx = len({d.coords[0] for d in mesh.devices.flat})
    ny = len({d.coords[1] for d in mesh.devices.flat})
    sub = Mesh(
        mesh.devices.reshape(nx, embed // nx, ny, hidden // ny),
        ("ex", "ec", "hy", "hz"),
    )
    rows = P(("hy", "hz"), EMBED)
    weights = P(EMBED, ("hy", "hz"))
    placed = (rows, weights, weights, rows)
    return jax.shard_map(
        on_device, mesh=sub, in_specs=placed, out_specs=rows, check_vma=False
    )
```

```python
import jax
import jax.numpy as jnp
from jax import lax
from jax.sharding import Mesh, PartitionSpec as P

EMBED = ("ex", "ec")


def ring_rs(x, axis, n):
    k = lax.axis_index(axis)
    xs = x.reshape((n, x.shape[0] // n) + x.shape[1:])
    half = x.shape[-1] // 2
    a, b = xs[..., :half], xs[..., half:]
    take = lambda arr, i: lax.dynamic_index_in_dim(arr, i % n, 0, keepdims=False)
    fwd = [(i, (i + 1) % n) for i in range(n)]
    bwd = [(i, (i - 1) % n) for i in range(n)]
    acc_a = take(a, k - 1)
    acc_b = take(b, k + 1)
    for s in range(n - 1):
        acc_a = lax.ppermute(acc_a, axis, fwd) + take(a, k - s - 2)
        acc_b = lax.ppermute(acc_b, axis, bwd) + take(b, k + s + 2)
    return jnp.concatenate([acc_a, acc_b], axis=-1)


def ring_ag(x, axis, n, f=lambda v: v):
    k = lax.axis_index(axis)
    fwd = [(i, (i + 1) % n) for i in range(n)]
    bwd = [(i, (i - 1) % n) for i in range(n)]
    nf = n // 2
    own = f(x)
    out = jnp.zeros((n,) + own.shape, own.dtype)
    put = lambda out, v, i: lax.dynamic_update_index_in_dim(out, f(v), i % n, 0)
    out = lax.dynamic_update_index_in_dim(out, own, k, 0)
    buf = x
    for s in range(nf):
        buf = lax.ppermute(buf, axis, fwd)
        out = put(out, buf, k - 1 - s)
    buf = x
    for s in range(n - 1 - nf):
        buf = lax.ppermute(buf, axis, bwd)
        out = put(out, buf, k + 1 + s)
    return out.reshape((n * own.shape[0],) + own.shape[1:])


def embed_rs(x):
    ec = lax.axis_index("ec")
    ncore = lax.psum(1, "ec")
    nx = lax.psum(1, "ex")
    xs = x.reshape((nx, ncore, x.shape[0] // (nx * ncore)) + x.shape[1:])
    mine = lax.dynamic_index_in_dim(xs, ec, 1, keepdims=False)
    other = lax.dynamic_index_in_dim(xs, 1 - ec, 1, keepdims=False)
    got = lax.ppermute(other, "ec", [(0, 1), (1, 0)])
    y = (mine + got).reshape((-1,) + x.shape[1:])
    return ring_rs(y, "ex", nx)


def on_device(rows_in, gate_weight, up_weight, down_weight):
    width = gate_weight.shape[1]
    ny = lax.psum(1, "hy")
    nz = lax.psum(1, "hz")
    partial_value = ring_ag(
        ring_ag(rows_in, "hy", ny),
        "hz",
        nz,
        lambda v: jnp.concatenate(
            [
                jnp.dot(v, gate_weight, preferred_element_type=jnp.float32),
                jnp.dot(v, up_weight, preferred_element_type=jnp.float32),
            ],
            axis=1,
        ),
    )
    summed = embed_rs(partial_value)
    activated = (jax.nn.silu(summed[:, :width]) * summed[:, width:]).astype(jnp.bfloat16)
    activated = lax.all_gather(activated, EMBED, axis=0, tiled=True)
    partial_out = jnp.dot(activated, down_weight, preferred_element_type=jnp.float32)
    pieces = partial_out.astype(jnp.bfloat16).reshape(
        (ny * nz, partial_out.shape[0] // (ny * nz)) + partial_out.shape[1:]
    )
    pieces = lax.all_to_all(pieces, ("hz", "hy"), 0, 0, tiled=True)
    totals = pieces.astype(jnp.float32).sum(axis=0)
    return totals.astype(jnp.bfloat16)


def solution(mesh):
    embed, hidden = mesh.shape["embed"], mesh.shape["hidden"]
    nx = len({d.coords[0] for d in mesh.devices.flat})
    ny = len({d.coords[1] for d in mesh.devices.flat})
    sub = Mesh(
        mesh.devices.reshape(nx, embed // nx, ny, hidden // ny),
        ("ex", "ec", "hy", "hz"),
    )
    rows = P(("hy", "hz"), EMBED)
    weights = P(EMBED, ("hy", "hz"))
    placed = (rows, weights, weights, rows)
    return jax.shard_map(
        on_device, mesh=sub, in_specs=placed, out_specs=rows, check_vma=False
    )
```

```python
import jax
import jax.numpy as jnp
from jax import lax
from jax.sharding import Mesh, PartitionSpec as P

EMBED = ("ex", "ec")


def ring_rs(x, axis, n):
    k = lax.axis_index(axis)
    xs = x.reshape((n, x.shape[0] // n) + x.shape[1:])
    half = x.shape[-1] // 2
    a, b = xs[..., :half], xs[..., half:]
    take = lambda arr, i: lax.dynamic_index_in_dim(arr, i % n, 0, keepdims=False)
    fwd = [(i, (i + 1) % n) for i in range(n)]
    bwd = [(i, (i - 1) % n) for i in range(n)]
    acc_a = take(a, k - 1)
    acc_b = take(b, k + 1)
    for s in range(n - 1):
        acc_a = lax.ppermute(acc_a, axis, fwd) + take(a, k - s - 2)
        acc_b = lax.ppermute(acc_b, axis, bwd) + take(b, k + s + 2)
    return jnp.concatenate([acc_a, acc_b], axis=-1)


def ring_ag(x, axis, n, f=lambda v: v):
    k = lax.axis_index(axis)
    fwd = [(i, (i + 1) % n) for i in range(n)]
    bwd = [(i, (i - 1) % n) for i in range(n)]
    nf = n // 2
    own = f(x)
    out = jnp.zeros((n,) + own.shape, own.dtype)
    put = lambda out, v, i: lax.dynamic_update_index_in_dim(out, f(v), i % n, 0)
    out = lax.dynamic_update_index_in_dim(out, own, k, 0)
    buf = x
    for s in range(nf):
        buf = lax.ppermute(buf, axis, fwd)
        out = put(out, buf, k - 1 - s)
    buf = x
    for s in range(n - 1 - nf):
        buf = lax.ppermute(buf, axis, bwd)
        out = put(out, buf, k + 1 + s)
    return out.reshape((n * own.shape[0],) + own.shape[1:])


def ring_rs2(x, axis, n, chunk_axis, send_dtype):
    k = lax.axis_index(axis)
    take = lambda i: lax.dynamic_index_in_dim(
        x, i % n, chunk_axis, keepdims=False
    ).astype(jnp.float32)
    fwd = [(i, (i + 1) % n) for i in range(n)]
    bwd = [(i, (i - 1) % n) for i in range(n)]
    nf = n // 2
    nb = n - 1 - nf
    total = take(k)
    acc = take(k + nf)
    for s in range(nf):
        acc = lax.ppermute(acc.astype(send_dtype), axis, fwd).astype(jnp.float32)
        if s < nf - 1:
            acc = acc + take(k + nf - s - 1)
    total = total + acc
    if nb:
        acc = take(k - nb)
        for s in range(nb):
            acc = lax.ppermute(acc.astype(send_dtype), axis, bwd).astype(jnp.float32)
            if s < nb - 1:
                acc = acc + take(k - nb + s + 1)
        total = total + acc
    return total


def embed_rs(x):
    ec = lax.axis_index("ec")
    ncore = lax.psum(1, "ec")
    nx = lax.psum(1, "ex")
    xs = x.reshape((nx, ncore, x.shape[0] // (nx * ncore)) + x.shape[1:])
    mine = lax.dynamic_index_in_dim(xs, ec, 1, keepdims=False)
    other = lax.dynamic_index_in_dim(xs, 1 - ec, 1, keepdims=False)
    got = lax.ppermute(other, "ec", [(0, 1), (1, 0)])
    y = (mine + got).reshape((-1,) + x.shape[1:])
    return ring_rs(y, "ex", nx)


def on_device(rows_in, gate_weight, up_weight, down_weight):
    width = gate_weight.shape[1]
    ny = lax.psum(1, "hy")
    nz = lax.psum(1, "hz")
    partial_value = ring_ag(
        ring_ag(rows_in, "hy", ny),
        "hz",
        nz,
        lambda v: jnp.concatenate(
            [
                jnp.dot(v, gate_weight, preferred_element_type=jnp.float32),
                jnp.dot(v, up_weight, preferred_element_type=jnp.float32),
            ],
            axis=1,
        ),
    )
    summed = embed_rs(partial_value)
    activated = (jax.nn.silu(summed[:, :width]) * summed[:, width:]).astype(jnp.bfloat16)
    activated = lax.all_gather(activated, EMBED, axis=0, tiled=True)
    partial_out = jnp.dot(activated, down_weight, preferred_element_type=jnp.float32)
    blocks = partial_out.reshape(
        (nz, ny, partial_out.shape[0] // (ny * nz)) + partial_out.shape[1:]
    )
    totals = ring_rs2(blocks, "hy", ny, 1, jnp.bfloat16)
    totals = ring_rs2(totals, "hz", nz, 0, jnp.float32)
    return totals.astype(jnp.bfloat16)


def solution(mesh):
    embed, hidden = mesh.shape["embed"], mesh.shape["hidden"]
    nx = len({d.coords[0] for d in mesh.devices.flat})
    ny = len({d.coords[1] for d in mesh.devices.flat})
    sub = Mesh(
        mesh.devices.reshape(nx, embed // nx, ny, hidden // ny),
        ("ex", "ec", "hy", "hz"),
    )
    rows = P(("hy", "hz"), EMBED)
    weights = P(EMBED, ("hy", "hz"))
    placed = (rows, weights, weights, rows)
    return jax.shard_map(
        on_device, mesh=sub, in_specs=placed, out_specs=rows, check_vma=False
    )
```

```python
import jax
import jax.numpy as jnp
from jax import lax
from jax.sharding import Mesh, PartitionSpec as P

EMBED = ("ex", "ec")


def ring_rs(x, axis, n):
    k = lax.axis_index(axis)
    xs = x.reshape((n, x.shape[0] // n) + x.shape[1:])
    half = x.shape[-1] // 2
    a, b = xs[..., :half], xs[..., half:]
    take = lambda arr, i: lax.dynamic_index_in_dim(arr, i % n, 0, keepdims=False)
    fwd = [(i, (i + 1) % n) for i in range(n)]
    bwd = [(i, (i - 1) % n) for i in range(n)]
    acc_a = take(a, k - 1)
    acc_b = take(b, k + 1)
    for s in range(n - 1):
        acc_a = lax.ppermute(acc_a, axis, fwd) + take(a, k - s - 2)
        acc_b = lax.ppermute(acc_b, axis, bwd) + take(b, k + s + 2)
    return jnp.concatenate([acc_a, acc_b], axis=-1)


def ring_ag(x, axis, n, f=lambda v: v):
    k = lax.axis_index(axis)
    fwd = [(i, (i + 1) % n) for i in range(n)]
    bwd = [(i, (i - 1) % n) for i in range(n)]
    nf = n // 2
    own = f(x)
    out = jnp.zeros((n,) + own.shape, own.dtype)
    put = lambda out, v, i: lax.dynamic_update_index_in_dim(out, f(v), i % n, 0)
    out = lax.dynamic_update_index_in_dim(out, own, k, 0)
    buf = x
    for s in range(nf):
        buf = lax.ppermute(buf, axis, fwd)
        out = put(out, buf, k - 1 - s)
    buf = x
    for s in range(n - 1 - nf):
        buf = lax.ppermute(buf, axis, bwd)
        out = put(out, buf, k + 1 + s)
    return out.reshape((n * own.shape[0],) + own.shape[1:])


def ring_rs2(x, axis, n, chunk_axis, send_dtype):
    k = lax.axis_index(axis)
    take = lambda i: lax.dynamic_index_in_dim(
        x, i % n, chunk_axis, keepdims=False
    ).astype(jnp.float32)
    fwd = [(i, (i + 1) % n) for i in range(n)]
    bwd = [(i, (i - 1) % n) for i in range(n)]
    nf = n // 2
    nb = n - 1 - nf
    total = take(k)
    acc = take(k + nf)
    for s in range(nf):
        acc = lax.ppermute(acc.astype(send_dtype), axis, fwd).astype(jnp.float32)
        if s < nf - 1:
            acc = acc + take(k + nf - s - 1)
    total = total + acc
    if nb:
        acc = take(k - nb)
        for s in range(nb):
            acc = lax.ppermute(acc.astype(send_dtype), axis, bwd).astype(jnp.float32)
            if s < nb - 1:
                acc = acc + take(k - nb + s + 1)
        total = total + acc
    return total


def embed_rs(x):
    ec = lax.axis_index("ec")
    ncore = lax.psum(1, "ec")
    nx = lax.psum(1, "ex")
    xs = x.reshape((nx, ncore, x.shape[0] // (nx * ncore)) + x.shape[1:])
    mine = lax.dynamic_index_in_dim(xs, ec, 1, keepdims=False)
    other = lax.dynamic_index_in_dim(xs, 1 - ec, 1, keepdims=False)
    got = lax.ppermute(other, "ec", [(0, 1), (1, 0)])
    y = (mine + got).reshape((-1,) + x.shape[1:])
    return ring_rs(y, "ex", nx)


def on_device(rows_in, gate_weight, up_weight, down_weight):
    width = gate_weight.shape[1]
    ny = lax.psum(1, "hy")
    nz = lax.psum(1, "hz")
    partial_value = ring_ag(
        ring_ag(rows_in, "hy", ny),
        "hz",
        nz,
        lambda v: jnp.concatenate(
            [
                jnp.dot(v, gate_weight, preferred_element_type=jnp.float32),
                jnp.dot(v, up_weight, preferred_element_type=jnp.float32),
            ],
            axis=1,
        ),
    )
    summed = embed_rs(partial_value)
    activated = (jax.nn.silu(summed[:, :width]) * summed[:, width:]).astype(jnp.bfloat16)
    activated = lax.all_gather(activated, EMBED, axis=0, tiled=True)
    partial_out = jnp.dot(activated, down_weight, preferred_element_type=jnp.float32)
    blocks = partial_out.reshape((nz, -1) + partial_out.shape[1:])
    totals = ring_rs2(blocks, "hz", nz, 0, jnp.bfloat16)
    totals = totals.reshape((ny, -1) + totals.shape[1:])
    totals = ring_rs2(totals, "hy", ny, 0, jnp.float32)
    return totals.astype(jnp.bfloat16)


def solution(mesh):
    embed, hidden = mesh.shape["embed"], mesh.shape["hidden"]
    nx = len({d.coords[0] for d in mesh.devices.flat})
    ny = len({d.coords[1] for d in mesh.devices.flat})
    sub = Mesh(
        mesh.devices.reshape(nx, embed // nx, ny, hidden // ny),
        ("ex", "ec", "hy", "hz"),
    )
    rows = P(("hy", "hz"), EMBED)
    weights = P(EMBED, ("hy", "hz"))
    placed = (rows, weights, weights, rows)
    return jax.shard_map(
        on_device, mesh=sub, in_specs=placed, out_specs=rows, check_vma=False
    )
```

```python
import jax
import jax.numpy as jnp
from jax import lax
from jax.sharding import Mesh, PartitionSpec as P

EMBED = ("ex", "ec")


def ring_ag(x, axis, n, f=lambda v: v):
    k = lax.axis_index(axis)
    fwd = [(i, (i + 1) % n) for i in range(n)]
    bwd = [(i, (i - 1) % n) for i in range(n)]
    nf = n // 2
    own = f(x)
    out = jnp.zeros((n,) + own.shape, own.dtype)
    put = lambda out, v, i: lax.dynamic_update_index_in_dim(out, f(v), i % n, 0)
    out = lax.dynamic_update_index_in_dim(out, own, k, 0)
    buf = x
    for s in range(nf):
        buf = lax.ppermute(buf, axis, fwd)
        out = put(out, buf, k - 1 - s)
    buf = x
    for s in range(n - 1 - nf):
        buf = lax.ppermute(buf, axis, bwd)
        out = put(out, buf, k + 1 + s)
    return out.reshape((n * own.shape[0],) + own.shape[1:])


def ring_rs_bal(take, axis, n, send_dtype):
    k = lax.axis_index(axis)
    get = lambda i: take(i % n).astype(jnp.float32)
    fwd = [(i, (i + 1) % n) for i in range(n)]
    bwd = [(i, (i - 1) % n) for i in range(n)]
    nf = n // 2
    own = get(k)
    h = own.shape[-1] // 2

    def side(perm, sign, cols):
        far = get(k + sign * nf)
        acc = far[..., :h] if cols == 0 else far[..., h:]
        for s in range(nf):
            got = lax.ppermute(acc.astype(send_dtype), axis, perm).astype(jnp.float32)
            if s == 0:
                if nf == 1:
                    return got
                acc = get(k + sign * (nf - 1))
                pad = [(0, 0)] * (got.ndim - 1) + ([(0, h)] if cols == 0 else [(h, 0)])
                acc = acc + jnp.pad(got, pad)
            elif s < nf - 1:
                acc = get(k + sign * (nf - 1 - s)) + got
            else:
                acc = got
        return acc

    cw = side(fwd, 1, 0)
    ccw = side(bwd, -1, 1)
    if nf == 1:
        return own + jnp.concatenate([cw, ccw], axis=-1)
    return own + cw + ccw


def embed_rs(x):
    ec = lax.axis_index("ec")
    ncore = lax.psum(1, "ec")
    nx = lax.psum(1, "ex")
    xs = x.reshape((nx, ncore, x.shape[0] // (nx * ncore)) + x.shape[1:])
    mine = lax.dynamic_index_in_dim(xs, ec, 1, keepdims=False)
    other = lax.dynamic_index_in_dim(xs, 1 - ec, 1, keepdims=False)
    got = lax.ppermute(other, "ec", [(0, 1), (1, 0)])
    y = mine + got
    return ring_rs_bal(
        lambda i: lax.dynamic_index_in_dim(y, i, 0, keepdims=False), "ex", nx, jnp.float32
    )


def on_device(rows_in, gate_weight, up_weight, down_weight):
    width = gate_weight.shape[1]
    ny = lax.psum(1, "hy")
    nz = lax.psum(1, "hz")
    partial_value = ring_ag(
        ring_ag(rows_in, "hy", ny),
        "hz",
        nz,
        lambda v: jnp.concatenate(
            [
                jnp.dot(v, gate_weight, preferred_element_type=jnp.float32),
                jnp.dot(v, up_weight, preferred_element_type=jnp.float32),
            ],
            axis=1,
        ),
    )
    summed = embed_rs(partial_value)
    activated = (jax.nn.silu(summed[:, :width]) * summed[:, width:]).astype(jnp.bfloat16)
    activated = lax.all_gather(activated, EMBED, axis=0, tiled=True)
    act_blocks = activated.reshape((nz, -1) + activated.shape[1:])
    project = lambda i: jnp.dot(
        lax.dynamic_index_in_dim(act_blocks, i, 0, keepdims=False),
        down_weight,
        preferred_element_type=jnp.float32,
    )
    totals = ring_rs_bal(project, "hz", nz, jnp.bfloat16)
    totals = totals.reshape((ny, -1) + totals.shape[1:])
    totals = ring_rs_bal(
        lambda i: lax.dynamic_index_in_dim(totals, i, 0, keepdims=False), "hy", ny, jnp.float32
    )
    return totals.astype(jnp.bfloat16)


def solution(mesh):
    embed, hidden = mesh.shape["embed"], mesh.shape["hidden"]
    nx = len({d.coords[0] for d in mesh.devices.flat})
    ny = len({d.coords[1] for d in mesh.devices.flat})
    sub = Mesh(
        mesh.devices.reshape(nx, embed // nx, ny, hidden // ny),
        ("ex", "ec", "hy", "hz"),
    )
    rows = P(("hy", "hz"), EMBED)
    weights = P(EMBED, ("hy", "hz"))
    placed = (rows, weights, weights, rows)
    return jax.shard_map(
        on_device, mesh=sub, in_specs=placed, out_specs=rows, check_vma=False
    )
```

```python
import jax
import jax.numpy as jnp
from jax import lax
from jax.sharding import Mesh, PartitionSpec as P

EMBED = ("ex", "ec")


def ring_ag(x, axis, n, f=lambda v: v):
    k = lax.axis_index(axis)
    fwd = [(i, (i + 1) % n) for i in range(n)]
    bwd = [(i, (i - 1) % n) for i in range(n)]
    nf = n // 2
    own = f(x)
    out = jnp.zeros((n,) + own.shape, own.dtype)
    put = lambda out, v, i: lax.dynamic_update_index_in_dim(out, f(v), i % n, 0)
    out = lax.dynamic_update_index_in_dim(out, own, k, 0)
    buf = x
    for s in range(nf):
        buf = lax.ppermute(buf, axis, fwd)
        out = put(out, buf, k - 1 - s)
    buf = x
    for s in range(n - 1 - nf):
        buf = lax.ppermute(buf, axis, bwd)
        out = put(out, buf, k + 1 + s)
    return out.reshape((n * own.shape[0],) + own.shape[1:])


def ring_rs_bal(take, axis, n, send_dtype):
    k = lax.axis_index(axis)
    get = lambda i: take(i % n).astype(jnp.float32)
    fwd = [(i, (i + 1) % n) for i in range(n)]
    bwd = [(i, (i - 1) % n) for i in range(n)]
    nf = n // 2
    own = get(k)
    h = own.shape[-1] // 2

    def side(perm, sign, cols):
        far = get(k + sign * nf)
        acc = far[..., :h] if cols == 0 else far[..., h:]
        for s in range(nf):
            got = lax.ppermute(acc.astype(send_dtype), axis, perm).astype(jnp.float32)
            if s == 0:
                if nf == 1:
                    return got
                acc = get(k + sign * (nf - 1))
                pad = [(0, 0)] * (got.ndim - 1) + ([(0, h)] if cols == 0 else [(h, 0)])
                acc = acc + jnp.pad(got, pad)
            elif s < nf - 1:
                acc = get(k + sign * (nf - 1 - s)) + got
            else:
                acc = got
        return acc

    cw = side(fwd, 1, 0)
    ccw = side(bwd, -1, 1)
    if nf == 1:
        return own + jnp.concatenate([cw, ccw], axis=-1)
    return own + cw + ccw


def embed_rs(x):
    ec = lax.axis_index("ec")
    ncore = lax.psum(1, "ec")
    nx = lax.psum(1, "ex")
    xs = x.reshape((nx, ncore, x.shape[0] // (nx * ncore)) + x.shape[1:])
    mine = lax.dynamic_index_in_dim(xs, ec, 1, keepdims=False)
    other = lax.dynamic_index_in_dim(xs, 1 - ec, 1, keepdims=False)
    got = lax.ppermute(other, "ec", [(0, 1), (1, 0)])
    y = mine + got
    return ring_rs_bal(
        lambda i: lax.dynamic_index_in_dim(y, i, 0, keepdims=False), "ex", nx, jnp.float32
    )


def on_device(rows_in, gate_weight, up_weight, down_weight):
    width = gate_weight.shape[1]
    ny = lax.psum(1, "hy")
    nz = lax.psum(1, "hz")
    both = jnp.concatenate([gate_weight, up_weight], axis=1)
    partial_value = ring_ag(
        ring_ag(rows_in, "hy", ny),
        "hz",
        nz,
        lambda v: jnp.dot(v, both, preferred_element_type=jnp.float32),
    )
    summed = embed_rs(partial_value)
    activated = (jax.nn.silu(summed[:, :width]) * summed[:, width:]).astype(jnp.bfloat16)
    activated = lax.all_gather(activated, EMBED, axis=0, tiled=True)
    act_blocks = activated.reshape((nz, -1) + activated.shape[1:])
    project = lambda i: jnp.dot(
        lax.dynamic_index_in_dim(act_blocks, i, 0, keepdims=False),
        down_weight,
        preferred_element_type=jnp.float32,
    )
    totals = ring_rs_bal(project, "hz", nz, jnp.bfloat16)
    totals = totals.reshape((ny, -1) + totals.shape[1:])
    totals = ring_rs_bal(
        lambda i: lax.dynamic_index_in_dim(totals, i, 0, keepdims=False), "hy", ny, jnp.float32
    )
    return totals.astype(jnp.bfloat16)


def solution(mesh):
    embed, hidden = mesh.shape["embed"], mesh.shape["hidden"]
    nx = len({d.coords[0] for d in mesh.devices.flat})
    ny = len({d.coords[1] for d in mesh.devices.flat})
    sub = Mesh(
        mesh.devices.reshape(nx, embed // nx, ny, hidden // ny),
        ("ex", "ec", "hy", "hz"),
    )
    rows = P(("hy", "hz"), EMBED)
    weights = P(EMBED, ("hy", "hz"))
    placed = (rows, weights, weights, rows)
    return jax.shard_map(
        on_device, mesh=sub, in_specs=placed, out_specs=rows, check_vma=False
    )
```

```python
import jax
import jax.numpy as jnp
from jax import lax
from jax.sharding import Mesh, PartitionSpec as P

EMBED = ("ex", "ec")


def ring_ag(x, axis, n, f=lambda v: v):
    k = lax.axis_index(axis)
    fwd = [(i, (i + 1) % n) for i in range(n)]
    bwd = [(i, (i - 1) % n) for i in range(n)]
    nf = n // 2
    own = f(x)
    out = jnp.zeros((n,) + own.shape, own.dtype)
    put = lambda out, v, i: lax.dynamic_update_index_in_dim(out, f(v), i % n, 0)
    out = lax.dynamic_update_index_in_dim(out, own, k, 0)
    buf = x
    for s in range(nf):
        buf = lax.ppermute(buf, axis, fwd)
        out = put(out, buf, k - 1 - s)
    buf = x
    for s in range(n - 1 - nf):
        buf = lax.ppermute(buf, axis, bwd)
        out = put(out, buf, k + 1 + s)
    return out.reshape((n * own.shape[0],) + own.shape[1:])


def ring_rs_bal(take, axis, n, send_dtype):
    k = lax.axis_index(axis)
    get = lambda i: take(i % n).astype(jnp.float32)
    fwd = [(i, (i + 1) % n) for i in range(n)]
    bwd = [(i, (i - 1) % n) for i in range(n)]
    nf = n // 2
    own = get(k)
    h = own.shape[-1] // 2

    far = get(k + nf)

    def side(perm, sign, cols):
        acc = far[..., :h] if cols == 0 else far[..., h:]
        for s in range(nf):
            got = lax.ppermute(acc.astype(send_dtype), axis, perm).astype(jnp.float32)
            if s == 0:
                if nf == 1:
                    return got
                acc = get(k + sign * (nf - 1))
                pad = [(0, 0)] * (got.ndim - 1) + ([(0, h)] if cols == 0 else [(h, 0)])
                acc = acc + jnp.pad(got, pad)
            elif s < nf - 1:
                acc = get(k + sign * (nf - 1 - s)) + got
            else:
                acc = got
        return acc

    cw = side(fwd, 1, 0)
    ccw = side(bwd, -1, 1)
    if nf == 1:
        return own + jnp.concatenate([cw, ccw], axis=-1)
    return own + cw + ccw


def embed_rs(x):
    ec = lax.axis_index("ec")
    ncore = lax.psum(1, "ec")
    nx = lax.psum(1, "ex")
    xs = x.reshape((nx, ncore, x.shape[0] // (nx * ncore)) + x.shape[1:])
    mine = lax.dynamic_index_in_dim(xs, ec, 1, keepdims=False)
    other = lax.dynamic_index_in_dim(xs, 1 - ec, 1, keepdims=False)
    got = lax.ppermute(other, "ec", [(0, 1), (1, 0)])
    y = mine + got
    return ring_rs_bal(
        lambda i: lax.dynamic_index_in_dim(y, i, 0, keepdims=False), "ex", nx, jnp.float32
    )


def on_device(rows_in, gate_weight, up_weight, down_weight):
    width = gate_weight.shape[1]
    ny = lax.psum(1, "hy")
    nz = lax.psum(1, "hz")
    partial_value = ring_ag(
        ring_ag(rows_in, "hy", ny),
        "hz",
        nz,
        lambda v: jnp.concatenate(
            [
                jnp.dot(v, gate_weight, preferred_element_type=jnp.float32),
                jnp.dot(v, up_weight, preferred_element_type=jnp.float32),
            ],
            axis=1,
        ),
    )
    summed = embed_rs(partial_value)
    activated = (jax.nn.silu(summed[:, :width]) * summed[:, width:]).astype(jnp.bfloat16)
    activated = lax.all_gather(activated, EMBED, axis=0, tiled=True)
    act_blocks = activated.reshape((nz, -1) + activated.shape[1:])
    project = lambda i: jnp.dot(
        lax.dynamic_index_in_dim(act_blocks, i, 0, keepdims=False),
        down_weight,
        preferred_element_type=jnp.float32,
    )
    totals = ring_rs_bal(project, "hz", nz, jnp.bfloat16)
    totals = totals.reshape((ny, -1) + totals.shape[1:])
    totals = ring_rs_bal(
        lambda i: lax.dynamic_index_in_dim(totals, i, 0, keepdims=False), "hy", ny, jnp.float32
    )
    return totals.astype(jnp.bfloat16)


def solution(mesh):
    embed, hidden = mesh.shape["embed"], mesh.shape["hidden"]
    nx = len({d.coords[0] for d in mesh.devices.flat})
    ny = len({d.coords[1] for d in mesh.devices.flat})
    sub = Mesh(
        mesh.devices.reshape(nx, embed // nx, ny, hidden // ny),
        ("ex", "ec", "hy", "hz"),
    )
    rows = P(("hy", "hz"), EMBED)
    weights = P(EMBED, ("hy", "hz"))
    placed = (rows, weights, weights, rows)
    return jax.shard_map(
        on_device, mesh=sub, in_specs=placed, out_specs=rows, check_vma=False
    )
```

```python
import jax
import jax.numpy as jnp
from jax import lax
from jax.sharding import Mesh, PartitionSpec as P

EMBED = ("ex", "ec")


def ring_ag(x, axis, n, f=lambda v: v):
    k = lax.axis_index(axis)
    fwd = [(i, (i + 1) % n) for i in range(n)]
    bwd = [(i, (i - 1) % n) for i in range(n)]
    nf = n // 2
    own = f(x)
    out = jnp.zeros((n,) + own.shape, own.dtype)
    put = lambda out, v, i: lax.dynamic_update_index_in_dim(out, f(v), i % n, 0)
    out = lax.dynamic_update_index_in_dim(out, own, k, 0)
    buf = x
    for s in range(nf):
        buf = lax.ppermute(buf, axis, fwd)
        out = put(out, buf, k - 1 - s)
    buf = x
    for s in range(n - 1 - nf):
        buf = lax.ppermute(buf, axis, bwd)
        out = put(out, buf, k + 1 + s)
    return out.reshape((n * own.shape[0],) + own.shape[1:])


def ring_rs_bal(take, axis, n, send_dtype):
    k = lax.axis_index(axis)
    get = lambda i: take(i % n).astype(jnp.float32)
    fwd = [(i, (i + 1) % n) for i in range(n)]
    bwd = [(i, (i - 1) % n) for i in range(n)]
    nf = n // 2
    own = get(k)
    h = own.shape[-1] // 2

    def side(perm, sign, cols):
        far = get(k + sign * nf)
        acc = far[..., :h] if cols == 0 else far[..., h:]
        for s in range(nf):
            got = lax.ppermute(acc.astype(send_dtype), axis, perm).astype(jnp.float32)
            if s == 0:
                if nf == 1:
                    return got
                acc = get(k + sign * (nf - 1))
                pad = [(0, 0)] * (got.ndim - 1) + ([(0, h)] if cols == 0 else [(h, 0)])
                acc = acc + jnp.pad(got, pad)
            elif s < nf - 1:
                acc = get(k + sign * (nf - 1 - s)) + got
            else:
                acc = got
        return acc

    cw = side(fwd, 1, 0)
    ccw = side(bwd, -1, 1)
    if nf == 1:
        return own + jnp.concatenate([cw, ccw], axis=-1)
    return own + cw + ccw


def embed_rs(x):
    ec = lax.axis_index("ec")
    ncore = lax.psum(1, "ec")
    nx = lax.psum(1, "ex")
    xs = x.reshape((nx, ncore, x.shape[0] // (nx * ncore)) + x.shape[1:])
    mine = lax.dynamic_index_in_dim(xs, ec, 1, keepdims=False)
    other = lax.dynamic_index_in_dim(xs, 1 - ec, 1, keepdims=False)
    got = lax.ppermute(other, "ec", [(0, 1), (1, 0)])
    y = mine + got
    return ring_rs_bal(
        lambda i: lax.dynamic_index_in_dim(y, i, 0, keepdims=False), "ex", nx, jnp.float32
    )


def on_device(rows_in, gate_weight, up_weight, down_weight):
    width = gate_weight.shape[1]
    ny = lax.psum(1, "hy")
    nz = lax.psum(1, "hz")
    partial_value = ring_ag(
        ring_ag(rows_in, "hy", ny),
        "hz",
        nz,
        lambda v: jnp.concatenate(
            [
                jnp.dot(v, gate_weight, preferred_element_type=jnp.float32),
                jnp.dot(v, up_weight, preferred_element_type=jnp.float32),
            ],
            axis=1,
        ),
    )
    summed = embed_rs(partial_value)
    activated = (jax.nn.silu(summed[:, :width]) * summed[:, width:]).astype(jnp.bfloat16)
    activated = lax.all_gather(activated, "ec", axis=0, tiled=True)
    activated = lax.all_gather(activated, "ex", axis=0, tiled=True)
    act_blocks = activated.reshape((nz, -1) + activated.shape[1:])
    project = lambda i: jnp.dot(
        lax.dynamic_index_in_dim(act_blocks, i, 0, keepdims=False),
        down_weight,
        preferred_element_type=jnp.float32,
    )
    totals = ring_rs_bal(project, "hz", nz, jnp.bfloat16)
    totals = totals.reshape((ny, -1) + totals.shape[1:])
    totals = ring_rs_bal(
        lambda i: lax.dynamic_index_in_dim(totals, i, 0, keepdims=False), "hy", ny, jnp.float32
    )
    return totals.astype(jnp.bfloat16)


def solution(mesh):
    embed, hidden = mesh.shape["embed"], mesh.shape["hidden"]
    nx = len({d.coords[0] for d in mesh.devices.flat})
    ny = len({d.coords[1] for d in mesh.devices.flat})
    sub = Mesh(
        mesh.devices.reshape(nx, embed // nx, ny, hidden // ny),
        ("ex", "ec", "hy", "hz"),
    )
    rows = P(("hy", "hz"), EMBED)
    weights = P(EMBED, ("hy", "hz"))
    placed = (rows, weights, weights, rows)
    return jax.shard_map(
        on_device, mesh=sub, in_specs=placed, out_specs=rows, check_vma=False
    )
```

```python
import jax
import jax.numpy as jnp
from jax import lax
from jax.sharding import Mesh, PartitionSpec as P

EMBED = ("ex", "ec")


def ring_ag(x, axis, n, f=lambda v: v):
    k = lax.axis_index(axis)
    fwd = [(i, (i + 1) % n) for i in range(n)]
    bwd = [(i, (i - 1) % n) for i in range(n)]
    nf = n // 2
    own = f(x)
    out = jnp.zeros((n,) + own.shape, own.dtype)
    put = lambda out, v, i: lax.dynamic_update_index_in_dim(out, f(v), i % n, 0)
    out = lax.dynamic_update_index_in_dim(out, own, k, 0)
    buf = x
    for s in range(nf):
        buf = lax.ppermute(buf, axis, fwd)
        out = put(out, buf, k - 1 - s)
    buf = x
    for s in range(n - 1 - nf):
        buf = lax.ppermute(buf, axis, bwd)
        out = put(out, buf, k + 1 + s)
    return out.reshape((n * own.shape[0],) + own.shape[1:])


def ring_rs_bal(take, axis, n, send_dtype):
    k = lax.axis_index(axis)
    get = lambda i: take(i % n).astype(jnp.float32)
    fwd = [(i, (i + 1) % n) for i in range(n)]
    bwd = [(i, (i - 1) % n) for i in range(n)]
    nf = n // 2
    own = get(k)
    h = own.shape[-1] // 2

    def side(perm, sign, cols):
        far = get(k + sign * nf)
        acc = far[..., :h] if cols == 0 else far[..., h:]
        for s in range(nf):
            got = lax.ppermute(acc.astype(send_dtype), axis, perm).astype(jnp.float32)
            if s == 0:
                if nf == 1:
                    return got
                acc = get(k + sign * (nf - 1))
                pad = [(0, 0)] * (got.ndim - 1) + ([(0, h)] if cols == 0 else [(h, 0)])
                acc = acc + jnp.pad(got, pad)
            elif s < nf - 1:
                acc = get(k + sign * (nf - 1 - s)) + got
            else:
                acc = got
        return acc

    cw = side(fwd, 1, 0)
    ccw = side(bwd, -1, 1)
    if nf == 1:
        return own + jnp.concatenate([cw, ccw], axis=-1)
    return own + cw + ccw


def embed_rs(x):
    ec = lax.axis_index("ec")
    ncore = lax.psum(1, "ec")
    nx = lax.psum(1, "ex")
    xs = x.reshape((nx, ncore, x.shape[0] // (nx * ncore)) + x.shape[1:])
    mine = lax.dynamic_index_in_dim(xs, ec, 1, keepdims=False)
    other = lax.dynamic_index_in_dim(xs, 1 - ec, 1, keepdims=False)
    got = lax.ppermute(other, "ec", [(0, 1), (1, 0)])
    y = mine + got
    return ring_rs_bal(
        lambda i: lax.dynamic_index_in_dim(y, i, 0, keepdims=False), "ex", nx, jnp.float32
    )


def on_device(rows_in, gate_weight, up_weight, down_weight):
    width = gate_weight.shape[1]
    ny = lax.psum(1, "hy")
    nz = lax.psum(1, "hz")
    partial_value = ring_ag(
        ring_ag(rows_in, "hy", ny),
        "hz",
        nz,
        lambda v: jnp.concatenate(
            [
                jnp.dot(v, gate_weight, preferred_element_type=jnp.float32),
                jnp.dot(v, up_weight, preferred_element_type=jnp.float32),
            ],
            axis=1,
        ),
    )
    summed = embed_rs(partial_value)
    activated = (jax.nn.silu(summed[:, :width]) * summed[:, width:]).astype(jnp.bfloat16)
    activated = lax.all_gather(activated, EMBED, axis=0, tiled=True)
    act_blocks = activated.reshape((nz, -1) + activated.shape[1:])
    project = lambda i: jnp.dot(
        lax.dynamic_index_in_dim(act_blocks, i, 0, keepdims=False),
        down_weight,
        preferred_element_type=jnp.float32,
    )
    totals = ring_rs_bal(project, "hz", nz, jnp.bfloat16)
    totals = totals.reshape((ny, -1) + totals.shape[1:])
    totals = ring_rs_bal(
        lambda i: lax.dynamic_index_in_dim(totals, i, 0, keepdims=False), "hy", ny, jnp.bfloat16
    )
    return totals.astype(jnp.bfloat16)


def solution(mesh):
    embed, hidden = mesh.shape["embed"], mesh.shape["hidden"]
    nx = len({d.coords[0] for d in mesh.devices.flat})
    ny = len({d.coords[1] for d in mesh.devices.flat})
    sub = Mesh(
        mesh.devices.reshape(nx, embed // nx, ny, hidden // ny),
        ("ex", "ec", "hy", "hz"),
    )
    rows = P(("hy", "hz"), EMBED)
    weights = P(EMBED, ("hy", "hz"))
    placed = (rows, weights, weights, rows)
    return jax.shard_map(
        on_device, mesh=sub, in_specs=placed, out_specs=rows, check_vma=False
    )
```

```python
import jax
import jax.numpy as jnp
from jax import lax
from jax.sharding import Mesh, PartitionSpec as P

EMBED = ("ex", "ec")


def ring_ag(x, axis, n, f=lambda v: v):
    k = lax.axis_index(axis)
    fwd = [(i, (i + 1) % n) for i in range(n)]
    bwd = [(i, (i - 1) % n) for i in range(n)]
    nf = n // 2
    own = f(x)
    out = jnp.zeros((n,) + own.shape, own.dtype)
    put = lambda out, v, i: lax.dynamic_update_index_in_dim(out, f(v), i % n, 0)
    out = lax.dynamic_update_index_in_dim(out, own, k, 0)
    buf = x
    for s in range(nf):
        buf = lax.ppermute(buf, axis, fwd)
        out = put(out, buf, k - 1 - s)
    buf = x
    for s in range(n - 1 - nf):
        buf = lax.ppermute(buf, axis, bwd)
        out = put(out, buf, k + 1 + s)
    return out.reshape((n * own.shape[0],) + own.shape[1:])


def ring_rs_bal(take, axis, n, send_dtype):
    k = lax.axis_index(axis)
    get = lambda i: take(i % n).astype(jnp.float32)
    fwd = [(i, (i + 1) % n) for i in range(n)]
    bwd = [(i, (i - 1) % n) for i in range(n)]
    nf = n // 2
    own = get(k)
    h = own.shape[-1] // 2

    def side(perm, sign, cols):
        far = get(k + sign * nf)
        acc = far[..., :h] if cols == 0 else far[..., h:]
        for s in range(nf):
            got = lax.ppermute(acc.astype(send_dtype), axis, perm).astype(jnp.float32)
            if s == 0:
                if nf == 1:
                    return got
                acc = get(k + sign * (nf - 1))
                pad = [(0, 0)] * (got.ndim - 1) + ([(0, h)] if cols == 0 else [(h, 0)])
                acc = acc + jnp.pad(got, pad)
            elif s < nf - 1:
                acc = get(k + sign * (nf - 1 - s)) + got
            else:
                acc = got
        return acc

    cw = side(fwd, 1, 0)
    ccw = side(bwd, -1, 1)
    if nf == 1:
        return own + jnp.concatenate([cw, ccw], axis=-1)
    return own + cw + ccw


def embed_rs(x):
    ec = lax.axis_index("ec")
    ncore = lax.psum(1, "ec")
    nx = lax.psum(1, "ex")
    xs = x.reshape((nx, ncore, x.shape[0] // (nx * ncore)) + x.shape[1:])
    mine = lax.dynamic_index_in_dim(xs, ec, 1, keepdims=False)
    other = lax.dynamic_index_in_dim(xs, 1 - ec, 1, keepdims=False)
    got = lax.ppermute(other, "ec", [(0, 1), (1, 0)])
    y = mine + got
    return ring_rs_bal(
        lambda i: lax.dynamic_index_in_dim(y, i, 0, keepdims=False), "ex", nx, jnp.float32
    )


def on_device(rows_in, gate_weight, up_weight, down_weight):
    width = gate_weight.shape[1]
    ny = lax.psum(1, "hy")
    nz = lax.psum(1, "hz")
    piece = ring_ag(ring_ag(rows_in, "hy", ny), "hz", nz)
    gate_part = jnp.dot(piece, gate_weight, preferred_element_type=jnp.float32)
    up_part = jnp.dot(piece, up_weight, preferred_element_type=jnp.float32)
    partial_value = jnp.concatenate([gate_part, up_part], axis=1)
    summed = embed_rs(partial_value)
    activated = (jax.nn.silu(summed[:, :width]) * summed[:, width:]).astype(jnp.bfloat16)
    activated = ring_ag(ring_ag(activated, "ec", lax.psum(1, "ec")), "ex", lax.psum(1, "ex"))
    act_blocks = activated.reshape((nz, -1) + activated.shape[1:])
    project = lambda i: jnp.dot(
        lax.dynamic_index_in_dim(act_blocks, i, 0, keepdims=False),
        down_weight,
        preferred_element_type=jnp.float32,
    )
    totals = ring_rs_bal(project, "hz", nz, jnp.bfloat16)
    totals = totals.reshape((ny, -1) + totals.shape[1:])
    totals = ring_rs_bal(
        lambda i: lax.dynamic_index_in_dim(totals, i, 0, keepdims=False), "hy", ny, jnp.bfloat16
    )
    return totals.astype(jnp.bfloat16)


def solution(mesh):
    embed, hidden = mesh.shape["embed"], mesh.shape["hidden"]
    nx = len({d.coords[0] for d in mesh.devices.flat})
    ny = len({d.coords[1] for d in mesh.devices.flat})
    sub = Mesh(
        mesh.devices.reshape(nx, embed // nx, ny, hidden // ny),
        ("ex", "ec", "hy", "hz"),
    )
    rows = P(("hy", "hz"), EMBED)
    weights = P(EMBED, ("hy", "hz"))
    placed = (rows, weights, weights, rows)
    return jax.shard_map(
        on_device, mesh=sub, in_specs=placed, out_specs=rows, check_vma=False
    )
```

```python
import jax
import jax.numpy as jnp
from jax import lax
from jax.sharding import Mesh, PartitionSpec as P

EMBED = ("ex", "ec")


def ring_ag(x, axis, n, f=lambda v: v):
    k = lax.axis_index(axis)
    fwd = [(i, (i + 1) % n) for i in range(n)]
    bwd = [(i, (i - 1) % n) for i in range(n)]
    nf = n // 2
    own = f(x)
    out = jnp.zeros((n,) + own.shape, own.dtype)
    put = lambda out, v, i: lax.dynamic_update_index_in_dim(out, f(v), i % n, 0)
    out = lax.dynamic_update_index_in_dim(out, own, k, 0)
    buf = x
    for s in range(nf):
        buf = lax.ppermute(buf, axis, fwd)
        out = put(out, buf, k - 1 - s)
    buf = x
    for s in range(n - 1 - nf):
        buf = lax.ppermute(buf, axis, bwd)
        out = put(out, buf, k + 1 + s)
    return out.reshape((n * own.shape[0],) + own.shape[1:])


def ring_rs_bal(take, axis, n, send_dtype):
    k = lax.axis_index(axis)
    get = lambda i: take(i % n).astype(jnp.float32)
    fwd = [(i, (i + 1) % n) for i in range(n)]
    bwd = [(i, (i - 1) % n) for i in range(n)]
    nf = n // 2
    own = get(k)
    h = own.shape[-1] // 2

    def side(perm, sign, cols):
        far = get(k + sign * nf)
        acc = far[..., :h] if cols == 0 else far[..., h:]
        for s in range(nf):
            got = lax.ppermute(acc.astype(send_dtype), axis, perm).astype(jnp.float32)
            if s == 0:
                if nf == 1:
                    return got
                acc = get(k + sign * (nf - 1))
                pad = [(0, 0)] * (got.ndim - 1) + ([(0, h)] if cols == 0 else [(h, 0)])
                acc = acc + jnp.pad(got, pad)
            elif s < nf - 1:
                acc = get(k + sign * (nf - 1 - s)) + got
            else:
                acc = got
        return acc

    cw = side(fwd, 1, 0)
    ccw = side(bwd, -1, 1)
    if nf == 1:
        return own + jnp.concatenate([cw, ccw], axis=-1)
    return own + cw + ccw


def embed_rs(x):
    ec = lax.axis_index("ec")
    ncore = lax.psum(1, "ec")
    nx = lax.psum(1, "ex")
    xs = x.reshape((nx, ncore, x.shape[0] // (nx * ncore)) + x.shape[1:])
    other = lax.dynamic_index_in_dim(xs, 1 - ec, 1, keepdims=False)
    got = lax.ppermute(other, "ec", [(0, 1), (1, 0)])
    piece = lambda i: lax.dynamic_index_in_dim(
        lax.dynamic_index_in_dim(xs, i, 0, keepdims=False), ec, 0, keepdims=False
    ) + lax.dynamic_index_in_dim(got, i, 0, keepdims=False)
    return ring_rs_bal(piece, "ex", nx, jnp.float32)


def on_device(rows_in, gate_weight, up_weight, down_weight):
    width = gate_weight.shape[1]
    ny = lax.psum(1, "hy")
    nz = lax.psum(1, "hz")
    partial_value = ring_ag(
        ring_ag(rows_in, "hy", ny),
        "hz",
        nz,
        lambda v: jnp.concatenate(
            [
                jnp.dot(v, gate_weight, preferred_element_type=jnp.float32),
                jnp.dot(v, up_weight, preferred_element_type=jnp.float32),
            ],
            axis=1,
        ),
    )
    summed = embed_rs(partial_value)
    activated = (jax.nn.silu(summed[:, :width]) * summed[:, width:]).astype(jnp.bfloat16)
    activated = lax.all_gather(activated, EMBED, axis=0, tiled=True)
    act_blocks = activated.reshape((nz, -1) + activated.shape[1:])
    project = lambda i: jnp.dot(
        lax.dynamic_index_in_dim(act_blocks, i, 0, keepdims=False),
        down_weight,
        preferred_element_type=jnp.float32,
    )
    totals = ring_rs_bal(project, "hz", nz, jnp.bfloat16)
    totals = totals.reshape((ny, -1) + totals.shape[1:])
    totals = ring_rs_bal(
        lambda i: lax.dynamic_index_in_dim(totals, i, 0, keepdims=False), "hy", ny, jnp.bfloat16
    )
    return totals.astype(jnp.bfloat16)


def solution(mesh):
    embed, hidden = mesh.shape["embed"], mesh.shape["hidden"]
    nx = len({d.coords[0] for d in mesh.devices.flat})
    ny = len({d.coords[1] for d in mesh.devices.flat})
    sub = Mesh(
        mesh.devices.reshape(nx, embed // nx, ny, hidden // ny),
        ("ex", "ec", "hy", "hz"),
    )
    rows = P(("hy", "hz"), EMBED)
    weights = P(EMBED, ("hy", "hz"))
    placed = (rows, weights, weights, rows)
    return jax.shard_map(
        on_device, mesh=sub, in_specs=placed, out_specs=rows, check_vma=False
    )
```

```python
import jax
import jax.numpy as jnp
from jax import lax
from jax.sharding import Mesh, PartitionSpec as P

EMBED = ("ex", "ec")


def ring_ag(x, axis, n, f=lambda v: v):
    k = lax.axis_index(axis)
    fwd = [(i, (i + 1) % n) for i in range(n)]
    bwd = [(i, (i - 1) % n) for i in range(n)]
    nf = n // 2
    own = f(x)
    out = jnp.zeros((n,) + own.shape, own.dtype)
    put = lambda out, v, i: lax.dynamic_update_index_in_dim(out, f(v), i % n, 0)
    out = lax.dynamic_update_index_in_dim(out, own, k, 0)
    buf = x
    for s in range(nf):
        buf = lax.ppermute(buf, axis, fwd)
        out = put(out, buf, k - 1 - s)
    buf = x
    for s in range(n - 1 - nf):
        buf = lax.ppermute(buf, axis, bwd)
        out = put(out, buf, k + 1 + s)
    return out.reshape((n * own.shape[0],) + own.shape[1:])


def ring_rs_bal(take, axis, n, send_dtype):
    k = lax.axis_index(axis)
    get = lambda i: take(i % n).astype(jnp.float32)
    fwd = [(i, (i + 1) % n) for i in range(n)]
    bwd = [(i, (i - 1) % n) for i in range(n)]
    nf = n // 2
    own = get(k)
    h = own.shape[-1] // 2

    def side(perm, sign, cols):
        far = get(k + sign * nf)
        acc = far[..., :h] if cols == 0 else far[..., h:]
        for s in range(nf):
            got = lax.ppermute(acc.astype(send_dtype), axis, perm).astype(jnp.float32)
            if s == 0:
                if nf == 1:
                    return got
                acc = get(k + sign * (nf - 1))
                pad = [(0, 0)] * (got.ndim - 1) + ([(0, h)] if cols == 0 else [(h, 0)])
                acc = acc + jnp.pad(got, pad)
            elif s < nf - 1:
                acc = get(k + sign * (nf - 1 - s)) + got
            else:
                acc = got
        return acc

    cw = side(fwd, 1, 0)
    ccw = side(bwd, -1, 1)
    if nf == 1:
        return own + jnp.concatenate([cw, ccw], axis=-1)
    return own + cw + ccw


def embed_rs(x):
    ec = lax.axis_index("ec")
    ncore = lax.psum(1, "ec")
    nx = lax.psum(1, "ex")
    xs = x.reshape((nx, ncore, x.shape[0] // (nx * ncore)) + x.shape[1:])
    mine = lax.dynamic_index_in_dim(xs, ec, 1, keepdims=False)
    other = lax.dynamic_index_in_dim(xs, 1 - ec, 1, keepdims=False)
    got = lax.ppermute(other, "ec", [(0, 1), (1, 0)])
    y = mine + got
    return ring_rs_bal(
        lambda i: lax.dynamic_index_in_dim(y, i, 0, keepdims=False), "ex", nx, jnp.float32
    )


def on_device(rows_in, gate_weight, up_weight, down_weight):
    width = gate_weight.shape[1]
    ny = lax.psum(1, "hy")
    nz = lax.psum(1, "hz")
    partial_value = ring_ag(
        ring_ag(rows_in, "hy", ny),
        "hz",
        nz,
        lambda v: jnp.concatenate(
            [
                jnp.dot(v, gate_weight, preferred_element_type=jnp.float32),
                jnp.dot(v, up_weight, preferred_element_type=jnp.float32),
            ],
            axis=1,
        ),
    )
    summed = embed_rs(partial_value)
    activated = (jax.nn.silu(summed[:, :width]) * summed[:, width:]).astype(jnp.bfloat16)
    activated = lax.all_gather(activated, EMBED, axis=0, tiled=True)
    act_blocks = activated.reshape((nz, -1) + activated.shape[1:])
    projected = jnp.einsum(
        "brh,hc->brc", act_blocks, down_weight, preferred_element_type=jnp.float32
    )
    project = lambda i: lax.dynamic_index_in_dim(projected, i, 0, keepdims=False)
    totals = ring_rs_bal(project, "hz", nz, jnp.bfloat16)
    totals = totals.reshape((ny, -1) + totals.shape[1:])
    totals = ring_rs_bal(
        lambda i: lax.dynamic_index_in_dim(totals, i, 0, keepdims=False), "hy", ny, jnp.bfloat16
    )
    return totals.astype(jnp.bfloat16)


def solution(mesh):
    embed, hidden = mesh.shape["embed"], mesh.shape["hidden"]
    nx = len({d.coords[0] for d in mesh.devices.flat})
    ny = len({d.coords[1] for d in mesh.devices.flat})
    sub = Mesh(
        mesh.devices.reshape(nx, embed // nx, ny, hidden // ny),
        ("ex", "ec", "hy", "hz"),
    )
    rows = P(("hy", "hz"), EMBED)
    weights = P(EMBED, ("hy", "hz"))
    placed = (rows, weights, weights, rows)
    return jax.shard_map(
        on_device, mesh=sub, in_specs=placed, out_specs=rows, check_vma=False
    )
```

```python
import jax
import jax.numpy as jnp
from jax import lax
from jax.sharding import Mesh, PartitionSpec as P

EMBED = ("ex", "ec")


def ring_ag(x, axis, n, f=lambda v: v):
    k = lax.axis_index(axis)
    fwd = [(i, (i + 1) % n) for i in range(n)]
    bwd = [(i, (i - 1) % n) for i in range(n)]
    nf = n // 2
    own = f(x)
    out = jnp.zeros((n,) + own.shape, own.dtype)
    put = lambda out, v, i: lax.dynamic_update_index_in_dim(out, f(v), i % n, 0)
    out = lax.dynamic_update_index_in_dim(out, own, k, 0)
    buf = x
    for s in range(nf):
        buf = lax.ppermute(buf, axis, fwd)
        out = put(out, buf, k - 1 - s)
    buf = x
    for s in range(n - 1 - nf):
        buf = lax.ppermute(buf, axis, bwd)
        out = put(out, buf, k + 1 + s)
    return out.reshape((n * own.shape[0],) + own.shape[1:])


def ring_rs_bal(take, axis, n, send_dtype):
    k = lax.axis_index(axis)
    get = lambda i: take(i % n).astype(jnp.float32)
    fwd = [(i, (i + 1) % n) for i in range(n)]
    bwd = [(i, (i - 1) % n) for i in range(n)]
    nf = n // 2
    own = get(k)
    h = own.shape[-1] // 2

    far = get(k + nf)

    def side(perm, sign, cols):
        acc = far[..., :h] if cols == 0 else far[..., h:]
        for s in range(nf):
            got = lax.ppermute(acc.astype(send_dtype), axis, perm).astype(jnp.float32)
            if s == 0:
                if nf == 1:
                    return got
                acc = get(k + sign * (nf - 1))
                pad = [(0, 0)] * (got.ndim - 1) + ([(0, h)] if cols == 0 else [(h, 0)])
                acc = acc + jnp.pad(got, pad)
            elif s < nf - 1:
                acc = get(k + sign * (nf - 1 - s)) + got
            else:
                acc = got
        return acc

    cw = side(fwd, 1, 0)
    ccw = side(bwd, -1, 1)
    if nf == 1:
        return own + jnp.concatenate([cw, ccw], axis=-1)
    return own + cw + ccw


def embed_rs(x):
    ec = lax.axis_index("ec")
    ncore = lax.psum(1, "ec")
    nx = lax.psum(1, "ex")
    xs = x.reshape((nx, ncore, x.shape[0] // (nx * ncore)) + x.shape[1:])
    mine = lax.dynamic_index_in_dim(xs, ec, 1, keepdims=False)
    other = lax.dynamic_index_in_dim(xs, 1 - ec, 1, keepdims=False)
    got = lax.ppermute(other, "ec", [(0, 1), (1, 0)])
    y = mine + got
    return ring_rs_bal(
        lambda i: lax.dynamic_index_in_dim(y, i, 0, keepdims=False), "ex", nx, jnp.float32
    )


def on_device(rows_in, gate_weight, up_weight, down_weight):
    width = gate_weight.shape[1]
    ny = lax.psum(1, "hy")
    nz = lax.psum(1, "hz")
    partial_value = ring_ag(
        ring_ag(rows_in, "hy", ny),
        "hz",
        nz,
        lambda v: jnp.concatenate(
            [
                jnp.dot(v, gate_weight, preferred_element_type=jnp.float32),
                jnp.dot(v, up_weight, preferred_element_type=jnp.float32),
            ],
            axis=1,
        ),
    )
    summed = embed_rs(partial_value)
    activated = (jax.nn.silu(summed[:, :width]) * summed[:, width:]).astype(jnp.bfloat16)
    activated = lax.all_gather(activated, EMBED, axis=0, tiled=True)
    act_blocks = activated.reshape((nz, -1) + activated.shape[1:])
    project = lambda i: jnp.dot(
        lax.dynamic_index_in_dim(act_blocks, i, 0, keepdims=False),
        down_weight,
        preferred_element_type=jnp.float32,
    )
    totals = ring_rs_bal(project, "hz", nz, jnp.bfloat16)
    totals = totals.reshape((ny, -1) + totals.shape[1:])
    totals = ring_rs_bal(
        lambda i: lax.dynamic_index_in_dim(totals, i, 0, keepdims=False), "hy", ny, jnp.bfloat16
    )
    return totals.astype(jnp.bfloat16)


def solution(mesh):
    embed, hidden = mesh.shape["embed"], mesh.shape["hidden"]
    nx = len({d.coords[0] for d in mesh.devices.flat})
    ny = len({d.coords[1] for d in mesh.devices.flat})
    sub = Mesh(
        mesh.devices.reshape(nx, embed // nx, ny, hidden // ny),
        ("ex", "ec", "hy", "hz"),
    )
    rows = P(("hy", "hz"), EMBED)
    weights = P(EMBED, ("hy", "hz"))
    placed = (rows, weights, weights, rows)
    return jax.shard_map(
        on_device, mesh=sub, in_specs=placed, out_specs=rows, check_vma=False
    )
```

```python
import jax
import jax.numpy as jnp
from jax import lax
from jax.sharding import Mesh, PartitionSpec as P

EMBED = ("ex", "ec")


def ring_ag(x, axis, n, f=lambda v: v):
    k = lax.axis_index(axis)
    fwd = [(i, (i + 1) % n) for i in range(n)]
    bwd = [(i, (i - 1) % n) for i in range(n)]
    nf = n // 2
    own = f(x)
    out = jnp.zeros((n,) + own.shape, own.dtype)
    put = lambda out, v, i: lax.dynamic_update_index_in_dim(out, f(v), i % n, 0)
    out = lax.dynamic_update_index_in_dim(out, own, k, 0)
    buf_f = buf_b = x
    for s in range(nf):
        if s < n - 1 - nf:
            buf_b = lax.ppermute(buf_b, axis, bwd)
        buf_f = lax.ppermute(buf_f, axis, fwd)
        if s < n - 1 - nf:
            out = put(out, buf_b, k + 1 + s)
        out = put(out, buf_f, k - 1 - s)
    return out.reshape((n * own.shape[0],) + own.shape[1:])


def ring_rs_bal(take, axis, n, send_dtype):
    k = lax.axis_index(axis)
    get = lambda i: take(i % n).astype(jnp.float32)
    fwd = [(i, (i + 1) % n) for i in range(n)]
    bwd = [(i, (i - 1) % n) for i in range(n)]
    nf = n // 2
    own = get(k)
    h = own.shape[-1] // 2

    def side(perm, sign, cols):
        far = get(k + sign * nf)
        acc = far[..., :h] if cols == 0 else far[..., h:]
        for s in range(nf):
            got = lax.ppermute(acc.astype(send_dtype), axis, perm).astype(jnp.float32)
            if s == 0:
                if nf == 1:
                    return got
                acc = get(k + sign * (nf - 1))
                pad = [(0, 0)] * (got.ndim - 1) + ([(0, h)] if cols == 0 else [(h, 0)])
                acc = acc + jnp.pad(got, pad)
            elif s < nf - 1:
                acc = get(k + sign * (nf - 1 - s)) + got
            else:
                acc = got
        return acc

    cw = side(fwd, 1, 0)
    ccw = side(bwd, -1, 1)
    if nf == 1:
        return own + jnp.concatenate([cw, ccw], axis=-1)
    return own + cw + ccw


def embed_rs(x):
    ec = lax.axis_index("ec")
    ncore = lax.psum(1, "ec")
    nx = lax.psum(1, "ex")
    xs = x.reshape((nx, ncore, x.shape[0] // (nx * ncore)) + x.shape[1:])
    mine = lax.dynamic_index_in_dim(xs, ec, 1, keepdims=False)
    other = lax.dynamic_index_in_dim(xs, 1 - ec, 1, keepdims=False)
    got = lax.ppermute(other, "ec", [(0, 1), (1, 0)])
    y = mine + got
    return ring_rs_bal(
        lambda i: lax.dynamic_index_in_dim(y, i, 0, keepdims=False), "ex", nx, jnp.float32
    )


def on_device(rows_in, gate_weight, up_weight, down_weight):
    width = gate_weight.shape[1]
    ny = lax.psum(1, "hy")
    nz = lax.psum(1, "hz")
    partial_value = ring_ag(
        ring_ag(rows_in, "hy", ny),
        "hz",
        nz,
        lambda v: jnp.concatenate(
            [
                jnp.dot(v, gate_weight, preferred_element_type=jnp.float32),
                jnp.dot(v, up_weight, preferred_element_type=jnp.float32),
            ],
            axis=1,
        ),
    )
    summed = embed_rs(partial_value)
    activated = (jax.nn.silu(summed[:, :width]) * summed[:, width:]).astype(jnp.bfloat16)
    activated = lax.all_gather(activated, EMBED, axis=0, tiled=True)
    act_blocks = activated.reshape((nz, -1) + activated.shape[1:])
    project = lambda i: jnp.dot(
        lax.dynamic_index_in_dim(act_blocks, i, 0, keepdims=False),
        down_weight,
        preferred_element_type=jnp.float32,
    )
    totals = ring_rs_bal(project, "hz", nz, jnp.bfloat16)
    totals = totals.reshape((ny, -1) + totals.shape[1:])
    totals = ring_rs_bal(
        lambda i: lax.dynamic_index_in_dim(totals, i, 0, keepdims=False), "hy", ny, jnp.bfloat16
    )
    return totals.astype(jnp.bfloat16)


def solution(mesh):
    embed, hidden = mesh.shape["embed"], mesh.shape["hidden"]
    nx = len({d.coords[0] for d in mesh.devices.flat})
    ny = len({d.coords[1] for d in mesh.devices.flat})
    sub = Mesh(
        mesh.devices.reshape(nx, embed // nx, ny, hidden // ny),
        ("ex", "ec", "hy", "hz"),
    )
    rows = P(("hy", "hz"), EMBED)
    weights = P(EMBED, ("hy", "hz"))
    placed = (rows, weights, weights, rows)
    return jax.shard_map(
        on_device, mesh=sub, in_specs=placed, out_specs=rows, check_vma=False
    )
```
